128 devices in a mesh: req: 8 (over x, core), mlp: 16 (over y, z).
Axes of the slice: x: 4, y: 4, z: 4, core: 2. Of those that a mesh axis runs over, the one named last changes fastest.
Arguments:
- hidden_in: bfloat16 [16384, 2560], P(('req', 'mlp')), may hold values from -6 to 6
- queries: bfloat16 [16384, 2048], P(('req', 'mlp')), may hold values from -120 to 120
- keys_new: bfloat16 [16384, 512], P(('req', 'mlp')), may hold values from -4.4 to 4.4
- values_new: bfloat16 [16384, 512], P(('req', 'mlp')), may hold values from -5 to 5
- keys_cache: bfloat16 [4096, 512], P('req'), may hold values from -4.4 to 4.4
- values_cache: bfloat16 [4096, 512], P('req'), may hold values from -5 to 5
- out_weight: bfloat16 [2048, 2560], replicated, may hold values from -0.375 to 0.375
- norm_gain: float32 [2560], replicated, may hold values from 0.25 to 1.75
- gate_weight: bfloat16 [2560, 9728], P(None, 'mlp'), may hold values from -0.125 to 0.125
- up_weight: bfloat16 [2560, 9728], P(None, 'mlp'), may hold values from -0.125 to 0.125
- down_weight: bfloat16 [9728, 2560], P('mlp'), may hold values from -0.0625 to 0.0625
- lengths: int32 [8, 16], P('req', 'mlp'), may hold values from 1 to 128, 1536 in all within a row
- slot_request: int32 [128], replicated, may hold values from 0 to 127, each once
- cache_group: int32 [8, 4], replicated, may hold values from 0 to 3, each once within a row
Outputs:
- output: bfloat16 [16384, 2560], P(('req', 'mlp'))
The draws below stay inside these ranges and needn't reach their ends.
Inputs may be any that keep to these rules, and one draw needn't show every extreme that they name: The 16 entries of one row of lengths sum to 1536, and one of them is 128. `slot_request`: each request appears in one slot. `cache_group`: each row names every group once.
All inputs are finite; a program needn't handle non-finite values. No bound on the sum of `lengths` on one device may be relied on, other than what follows from the above.
Results may differ from the reference program's by a relative error of at most 0.014.
Values may be sent and summed in bfloat16 or wider, within the bound.
No kernel may reach another device: no remote copies, remote signals or barrier semaphores. Data moves between devices by JAX's collectives and lax.ppermute only.
A program may use at most 128 MiB of HBM per device.

```python
import math
import jax
import jax.numpy as jnp
import numpy as np
from jax import lax

D = 2560
HEADS = 16
KVH = 4
HD = 128
FF = 9728
GROUPS = 4
TOK = 128
PREFIX = 1024
REQUESTS = 128
TOKENS = 16384
N_REQ = 8
N_MLP = 16


def draw_queries(key, part):
    base = jax.random.fold_in(key, 11)
    drawn = jnp.clip(2.0 * jax.random.normal(base, (TOKENS, HEADS * HD), jnp.float32), -8.0, 8.0)
    return drawn.astype(jnp.bfloat16)


def draw_keys_new(key, part):
    base = jax.random.fold_in(key, 12)
    drawn = jax.random.normal(base, (TOKENS, KVH * HD), jnp.float32)
    return jnp.clip(drawn, -4.375, 4.375).astype(jnp.bfloat16)


def draw_keys_cache(key, part):
    base = jax.random.fold_in(key, 13)
    total_rows = GROUPS * PREFIX
    drawn = jax.random.normal(base, (total_rows, KVH * HD), jnp.float32)
    return jnp.clip(drawn, -4.375, 4.375).astype(jnp.bfloat16)


def levels(stream_key, extent, pieces, low, high):
    gain, own = 1.0, jax.random.fold_in(stream_key, 6)
    for dim, parts in pieces:
        draws = jnp.exp(jax.random.uniform(jax.random.fold_in(own, dim), (parts,), jnp.float32, low / len(pieces), high / len(pieces)))
        gain = gain * jnp.repeat(draws, extent[dim] // parts).reshape([-1 if axis == dim else 1 for axis in range(len(extent))])
    return gain


def profile(count, total, reach, skew):
    loads = [(1 << 20) // math.isqrt(rank ** skew) + 1 for rank in range(2, count + 1)]
    rest, holding = total - reach - (count - 1), [1] * (count - 1)
    while rest > 0:
        free = [i for i in range(count - 1) if holding[i] < reach]
        mass, left = sum([loads[i] for i in free]), rest
        for i in free:
            extra = min(reach - holding[i], max(1, left * loads[i] // mass), rest)
            holding[i] = holding[i] + extra
            rest = rest - extra
    return np.array([reach] + holding)


def uneven(stream_key, amount, total, most, skew):
    if amount == 2:
        one = jax.random.randint(stream_key, (), max(1, total - most), min(most, total - 1) + 1)
        return jnp.stack([one, total - one])
    sizes = jnp.asarray(profile(amount, total, most, skew), jnp.int32)
    pairs = (amount - 1) // 2
    source_of, receiver = sizes[1:1 + 2 * pairs:2], sizes[2:2 + 2 * pairs:2]
    slack = jnp.minimum(source_of - 1, most - receiver)
    moved = jax.random.randint(jax.random.fold_in(stream_key, 1), (pairs,), 0, 1 << 20) % (slack + 1)
    sizes = sizes.at[1:1 + 2 * pairs:2].set(source_of - moved).at[2:2 + 2 * pairs:2].set(receiver + moved)
    return sizes[jax.random.permutation(jax.random.fold_in(stream_key, 2), amount)]


def gaussian(key, dims, scale, most, shards=(), kind=jnp.bfloat16):
    level = levels(key, dims, shards, -0.22, 0.18) if shards else 1.0
    array = jax.random.normal(key, dims, jnp.float32) * scale * level
    return jnp.minimum(jnp.maximum(array, -most), most).astype(kind)


def setup_inputs(seed: int = 0) -> dict:
    key_list = jax.random.split(jax.random.key(seed), 15)
    hidden_in = gaussian(key_list[0], (TOKENS, D), 1.0, 6.0, ((0, 128),))
    queries = draw_queries(jax.random.fold_in(key_list[14], 71), 0)
    keys_new = draw_keys_new(jax.random.fold_in(key_list[14], 71), 0)
    values_new = gaussian(key_list[3], (TOKENS, KVH * HD), 1.0, 5.0, ((0, 128),))
    keys_cache = draw_keys_cache(jax.random.fold_in(key_list[14], 71), 0)
    values_cache = gaussian(key_list[5], (GROUPS * PREFIX, KVH * HD), 1.0, 5.0, ((0, 8),))
    out_weight = gaussian(key_list[6], (HEADS * HD, D), (HEADS * HD // 8) ** -0.5, 0.375)
    norm_gain = jnp.clip(1.0 + 0.15 * jax.random.normal(key_list[7], (D,), jnp.float32), 0.25, 1.75)
    gate_weight = gaussian(key_list[8], (D, FF), D ** -0.5, 0.125, ((1, 16),))
    up_weight = gaussian(key_list[9], (D, FF), D ** -0.5, 0.125, ((1, 16),))
    down_weight = gaussian(key_list[10], (FF, D), FF ** -0.5, 0.0625, ((0, 16),))
    lengths = jax.vmap(lambda own: uneven(own, N_MLP, N_MLP * TOK * 3 // 4, TOK, 1))(jax.random.split(key_list[11], N_REQ)).reshape((N_REQ, N_MLP)).astype(jnp.int32)
    slot_request = jax.random.permutation(key_list[12], REQUESTS).astype(jnp.int32)
    cache_group = jax.vmap(lambda own: jax.random.permutation(own, GROUPS))(jax.random.split(key_list[13], N_REQ)).reshape((N_REQ, GROUPS)).astype(jnp.int32)
    return dict(hidden_in=hidden_in, queries=queries, keys_new=keys_new, values_new=values_new, keys_cache=keys_cache, values_cache=values_cache, out_weight=out_weight, norm_gain=norm_gain, gate_weight=gate_weight, up_weight=up_weight, down_weight=down_weight, lengths=lengths, slot_request=slot_request, cache_group=cache_group)


NEGATIVE = -1e+30
EPSILON = 1e-06

def attend_slot(query_block, key_rows, value_rows, allowed):
    row_count = query_block.shape[0]
    key_count = key_rows.shape[0]
    per_group = HEADS // KVH
    query_heads = query_block.astype(jnp.float32).reshape(row_count, KVH, per_group, HD)
    key_heads = key_rows.astype(jnp.float32).reshape(key_count, KVH, HD)
    value_heads = value_rows.astype(jnp.float32).reshape(key_count, KVH, HD)
    scores = jnp.einsum('tkgd,skd->kgts', query_heads, key_heads) * HD ** (-0.5)
    scores = jnp.where(allowed, scores, NEGATIVE)
    maxima = lax.optimization_barrier(jnp.max(scores, axis=3, keepdims=True))
    weights = jnp.exp(scores - maxima)
    totals = lax.optimization_barrier(jnp.sum(weights, axis=3))
    rounded = lax.optimization_barrier(weights.astype(jnp.bfloat16)).astype(jnp.float32)
    context = jnp.einsum('kgts,skd->tkgd', rounded, value_heads)
    context = context / jnp.transpose(totals, (2, 0, 1))[..., None]
    return context.reshape(row_count, HEADS * HD).astype(jnp.bfloat16)

def regroup(cache_rows, where_group):
    piece_rows = PREFIX // N_REQ
    slabs = cache_rows.reshape(N_REQ, GROUPS, piece_rows, KVH * HD)
    picked = jnp.take_along_axis(slabs, where_group[:, :, None, None], axis=1)
    return jnp.transpose(picked, (1, 0, 2, 3)).reshape(GROUPS, PREFIX, KVH * HD)

def reference(hidden_in, queries, keys_new, values_new, keys_cache, values_cache, out_weight, norm_gain, gate_weight, up_weight, down_weight, lengths, slot_request, cache_group):
    slots = N_REQ * N_MLP
    slot_group = slot_request // (slots // GROUPS)
    row_index = jnp.broadcast_to(jnp.arange(N_REQ, dtype=jnp.int32)[:, None], (N_REQ, GROUPS))
    sub_index = jnp.broadcast_to(jnp.arange(GROUPS, dtype=jnp.int32)[None, :], (N_REQ, GROUPS))
    where_group = jnp.zeros((N_REQ, GROUPS), jnp.int32).at[row_index, cache_group].set(sub_index)
    group_keys = regroup(keys_cache, where_group)
    group_values = regroup(values_cache, where_group)
    positions = jnp.arange(TOK, dtype=jnp.int32)
    allowed = jnp.concatenate([jnp.ones((TOK, PREFIX), jnp.bool_), positions[:, None] >= positions[None, :]], axis=1)

    def one_slot(slot_item):
        query_block, key_block, value_block, group_id = slot_item
        key_rows = jnp.concatenate([group_keys[group_id], key_block], axis=0)
        value_rows = jnp.concatenate([group_values[group_id], value_block], axis=0)
        return attend_slot(query_block, key_rows, value_rows, allowed)
    context = lax.map(one_slot, (queries.reshape(slots, TOK, HEADS * HD), keys_new.reshape(slots, TOK, KVH * HD), values_new.reshape(slots, TOK, KVH * HD), slot_group))
    context = context.reshape(slots * TOK, HEADS * HD)
    attended = jnp.dot(context, out_weight, preferred_element_type=jnp.float32)
    residual = (hidden_in.astype(jnp.float32) + attended).astype(jnp.bfloat16)
    widened = residual.astype(jnp.float32)
    normed = (widened * lax.rsqrt(lax.optimization_barrier(jnp.mean(widened * widened, axis=1, keepdims=True)) + EPSILON) * norm_gain[None, :]).astype(jnp.bfloat16)
    block_width = FF // N_MLP
    gate_blocks = gate_weight.reshape(D, N_MLP, block_width).transpose(1, 0, 2)
    up_blocks = up_weight.reshape(D, N_MLP, block_width).transpose(1, 0, 2)
    down_blocks = down_weight.reshape(N_MLP, block_width, D)

    def add_block(running, block_weights):
        gate_part, upward_part, down_part = block_weights
        gate_values = jnp.dot(normed, gate_part, preferred_element_type=jnp.float32)
        upward = jnp.dot(normed, upward_part, preferred_element_type=jnp.float32)
        hidden = (jax.nn.silu(gate_values) * upward).astype(jnp.bfloat16)
        block_term = jnp.dot(hidden, down_part, preferred_element_type=jnp.float32)
        rounded = lax.optimization_barrier(block_term.astype(jnp.bfloat16)).astype(jnp.float32)
        return (running + rounded, None)
    mixed = lax.scan(add_block, jnp.zeros((slots * TOK, D), jnp.float32), (gate_blocks, up_blocks, down_blocks))[0]
    result = residual.astype(jnp.float32) + mixed
    live_slot = (positions[None, :] < lengths.reshape(slots)[:, None]).reshape(slots * TOK, 1)
    return jnp.where(live_slot, result, 0.0).astype(jnp.bfloat16)
```

```python
import jax
import jax.numpy as jnp
from jax import lax
from jax.sharding import PartitionSpec as P

HEADS = 16
KVH = 4
HD = 128
GROUPS = 4


NEGATIVE = -1e30
EPSILON = 1e-06


def partial_attention(query_block, key_rows, value_rows, allowed):
    row_count = query_block.shape[0]
    key_count = key_rows.shape[0]
    per_group = HEADS // KVH
    query_heads = query_block.reshape(row_count, KVH, per_group, HD)
    key_heads = key_rows.reshape(key_count, KVH, HD)
    value_heads = value_rows.reshape(key_count, KVH, HD)
    scores = jnp.einsum(
        "tkgd,skd->kgts", query_heads, key_heads, preferred_element_type=jnp.float32
    ) * HD ** (-0.5)
    if allowed is not None:
        scores = jnp.where(allowed, scores, NEGATIVE)
    maxima = jnp.max(scores, axis=3)
    weights = jnp.exp(scores - maxima[..., None])
    totals = jnp.sum(weights, axis=3)
    context = jnp.einsum(
        "kgts,skd->tkgd",
        weights.astype(jnp.bfloat16),
        value_heads,
        preferred_element_type=jnp.float32,
    )
    context = context.reshape(row_count, HEADS * HD)
    maxima = jnp.transpose(maxima, (2, 0, 1)).reshape(row_count, HEADS)
    totals = jnp.transpose(totals, (2, 0, 1)).reshape(row_count, HEADS)
    return (context, maxima, totals)


def merge_pair(earlier, latest):
    context_early, maxima_early, totals_early = earlier
    context_late, maxima_late, totals_late = latest
    row_count = context_early.shape[0]
    highest = jnp.maximum(maxima_early, maxima_late)
    factor_early = jnp.exp(maxima_early - highest)
    factor_late = jnp.exp(maxima_late - highest)
    context = (
        context_early.reshape(row_count, HEADS, HD) * factor_early[..., None]
        + context_late.reshape(row_count, HEADS, HD) * factor_late[..., None]
    )
    return (
        context.reshape(row_count, HEADS * HD),
        highest,
        totals_early * factor_early + totals_late * factor_late,
    )


def shards(
    hidden_in,
    queries,
    keys_new,
    values_new,
    keys_cache,
    values_cache,
    out_weight,
    norm_gain,
    gate_weight,
    up_weight,
    down_weight,
    lengths,
    slot_request,
    cache_group,
):
    owners = lax.axis_size("req")
    columns = lax.axis_size("mlp")
    owner_index = lax.axis_index("req")
    column_index = lax.axis_index("mlp")
    tokens = queries.shape[0]
    width_kv = keys_cache.shape[1]
    piece_rows = keys_cache.shape[0] // GROUPS
    slot_group = slot_request // (slot_request.shape[0] // GROUPS)
    own_row = cache_group[owner_index]
    wanted = lax.dynamic_slice_in_dim(slot_group.reshape(owners, columns), column_index, 1, 1)[:, 0]
    group_ids = jnp.arange(GROUPS, dtype=jnp.int32)
    sub_block = jnp.sum(
        jnp.where(own_row[None, :] == wanted[:, None], group_ids[None, :], 0), axis=1
    )
    slab_keys = keys_cache.reshape(GROUPS, piece_rows, width_kv)
    slab_values = values_cache.reshape(GROUPS, piece_rows, width_kv)
    positions = jnp.arange(tokens, dtype=jnp.int32)
    causal = positions[:, None] >= positions[None, :]
    local_part = partial_attention(queries, keys_new, values_new, causal)
    slab_both = jnp.concatenate([slab_keys, slab_values], axis=2)
    send_both = jnp.take(slab_both, sub_block, axis=0)
    got_both = lax.all_to_all(send_both, "req", split_axis=0, concat_axis=0, tiled=True)
    got_keys = got_both[:, :, :width_kv]
    got_values = got_both[:, :, width_kv:]
    prefix_part = partial_attention(
        queries,
        got_keys.reshape(owners * piece_rows, width_kv),
        got_values.reshape(owners * piece_rows, width_kv),
        None,
    )
    context, highest, totals = merge_pair(local_part, prefix_part)
    context = context.reshape(tokens, HEADS, HD)
    context = (context / totals[..., None]).reshape(tokens, HEADS * HD).astype(jnp.bfloat16)
    attended = jnp.dot(context, out_weight, preferred_element_type=jnp.float32)
    residual = (hidden_in.astype(jnp.float32) + attended).astype(jnp.bfloat16)
    widened = residual.astype(jnp.float32)
    normed = (
        widened
        * lax.rsqrt(jnp.mean(widened * widened, axis=1, keepdims=True) + EPSILON)
        * norm_gain[None, :]
    ).astype(jnp.bfloat16)
    chunks = 2
    chunk_rows = tokens // chunks
    mixed_parts = []
    for part in range(chunks):
        own_rows = normed[part * chunk_rows:(part + 1) * chunk_rows]
        shard_rows = lax.all_gather(own_rows, "mlp", axis=0, tiled=True)
        gate_values = jnp.dot(shard_rows, gate_weight, preferred_element_type=jnp.float32)
        upward = jnp.dot(shard_rows, up_weight, preferred_element_type=jnp.float32)
        hidden = (jax.nn.silu(gate_values) * upward).astype(jnp.bfloat16)
        partial_terms = jnp.dot(hidden, down_weight, preferred_element_type=jnp.float32)
        mixed_parts.append(
            lax.psum_scatter(
                partial_terms.astype(jnp.bfloat16), "mlp", scatter_dimension=0, tiled=True
            )
        )
    mixed = jnp.concatenate(mixed_parts, axis=0).astype(jnp.float32)
    result = residual.astype(jnp.float32) + mixed
    live_slot = positions[:, None] < lengths[0, 0]
    return jnp.where(live_slot, result, 0.0).astype(jnp.bfloat16)


def solution(mesh):
    return jax.shard_map(
        shards,
        mesh=mesh,
        in_specs=(
            P(("req", "mlp"), None),
            P(("req", "mlp"), None),
            P(("req", "mlp"), None),
            P(("req", "mlp"), None),
            P("req", None),
            P("req", None),
            P(),
            P(),
            P(None, "mlp"),
            P(None, "mlp"),
            P("mlp", None),
            P("req", "mlp"),
            P(),
            P(),
        ),
        out_specs=P(("req", "mlp"), None),
        check_vma=False,
    )
```

```python
import jax
import jax.numpy as jnp
from jax import lax
from jax.sharding import PartitionSpec as P

HEADS = 16
KVH = 4
HD = 128
GROUPS = 4


NEGATIVE = -1e30
EPSILON = 1e-06


def full_attention(queries, key_rows, value_rows, allowed):
    row_count = queries.shape[0]
    per_group = HEADS // KVH
    outputs = []
    for head in range(KVH):
        query_heads = queries[:, head * per_group * HD:(head + 1) * per_group * HD].reshape(
            row_count, per_group, HD
        )
        key_head = key_rows[:, head * HD:(head + 1) * HD]
        value_head = value_rows[:, head * HD:(head + 1) * HD]
        scores = jnp.einsum(
            "tgd,sd->gts", query_heads, key_head, preferred_element_type=jnp.float32
        ) * HD ** (-0.5)
        scores = jnp.where(allowed[None], scores, NEGATIVE)
        maxima = jnp.max(scores, axis=2, keepdims=True)
        weights = jnp.exp(scores - maxima)
        totals = jnp.sum(weights, axis=2)
        context = jnp.einsum(
            "gts,sd->tgd",
            weights.astype(jnp.bfloat16),
            value_head,
            preferred_element_type=jnp.float32,
        )
        context = context / jnp.transpose(totals)[..., None]
        outputs.append(context.reshape(row_count, per_group * HD))
    return jnp.concatenate(outputs, axis=1).astype(jnp.bfloat16)


def shards(
    hidden_in,
    queries,
    keys_new,
    values_new,
    keys_cache,
    values_cache,
    out_weight,
    norm_gain,
    gate_weight,
    up_weight,
    down_weight,
    lengths,
    slot_request,
    cache_group,
):
    owners = lax.axis_size("req")
    columns = lax.axis_size("mlp")
    owner_index = lax.axis_index("req")
    column_index = lax.axis_index("mlp")
    tokens = queries.shape[0]
    width_kv = keys_cache.shape[1]
    piece_rows = keys_cache.shape[0] // GROUPS
    slot_group = slot_request // (slot_request.shape[0] // GROUPS)
    own_row = cache_group[owner_index]
    wanted = lax.dynamic_slice_in_dim(slot_group.reshape(owners, columns), column_index, 1, 1)[:, 0]
    group_ids = jnp.arange(GROUPS, dtype=jnp.int32)
    sub_block = jnp.sum(
        jnp.where(own_row[None, :] == wanted[:, None], group_ids[None, :], 0), axis=1
    )
    slab_both = jnp.concatenate(
        [keys_cache.reshape(GROUPS, piece_rows, width_kv), values_cache.reshape(GROUPS, piece_rows, width_kv)],
        axis=2,
    )
    pick = (sub_block[:, None] == group_ids[None, :])[:, :, None, None]
    send_both = jnp.sum(jnp.where(pick, slab_both[None], jnp.zeros((), slab_both.dtype)), axis=1)
    got_both = lax.all_to_all(send_both, "req", split_axis=0, concat_axis=0, tiled=True)
    got_both = got_both.reshape(owners * piece_rows, 2 * width_kv)
    key_rows = jnp.concatenate([got_both[:, :width_kv], keys_new], axis=0)
    value_rows = jnp.concatenate([got_both[:, width_kv:], values_new], axis=0)
    positions = jnp.arange(tokens, dtype=jnp.int32)
    causal = positions[:, None] >= positions[None, :]
    allowed = jnp.concatenate(
        [jnp.ones((tokens, owners * piece_rows), jnp.bool_), causal], axis=1
    )
    context = full_attention(queries, key_rows, value_rows, allowed)
    attended = jnp.dot(context, out_weight, preferred_element_type=jnp.float32)
    residual = (hidden_in.astype(jnp.float32) + attended).astype(jnp.bfloat16)
    widened = residual.astype(jnp.float32)
    normed = (
        widened
        * lax.rsqrt(jnp.mean(widened * widened, axis=1, keepdims=True) + EPSILON)
        * norm_gain[None, :]
    ).astype(jnp.bfloat16)
    shard_rows = lax.all_gather(normed, "mlp", axis=0, tiled=True)
    gate_values = jnp.dot(shard_rows, gate_weight, preferred_element_type=jnp.float32)
    upward = jnp.dot(shard_rows, up_weight, preferred_element_type=jnp.float32)
    hidden = (jax.nn.silu(gate_values) * upward).astype(jnp.bfloat16)
    partial_terms = jnp.dot(hidden, down_weight, preferred_element_type=jnp.float32)
    mixed = lax.psum_scatter(
        partial_terms.astype(jnp.bfloat16), "mlp", scatter_dimension=0, tiled=True
    ).astype(jnp.float32)
    result = residual.astype(jnp.float32) + mixed
    live_slot = positions[:, None] < lengths[0, 0]
    return jnp.where(live_slot, result, 0.0).astype(jnp.bfloat16)


def solution(mesh):
    return jax.shard_map(
        shards,
        mesh=mesh,
        in_specs=(
            P(("req", "mlp"), None),
            P(("req", "mlp"), None),
            P(("req", "mlp"), None),
            P(("req", "mlp"), None),
            P("req", None),
            P("req", None),
            P(),
            P(),
            P(None, "mlp"),
            P(None, "mlp"),
            P("mlp", None),
            P("req", "mlp"),
            P(),
            P(),
        ),
        out_specs=P(("req", "mlp"), None),
        check_vma=False,
    )
```

```python
import jax
import jax.numpy as jnp
from jax import lax
from jax.sharding import PartitionSpec as P

HEADS = 16
KVH = 4
HD = 128
GROUPS = 4


NEGATIVE = -1e30
EPSILON = 1e-06


def full_attention(queries, key_rows, value_rows, allowed):
    row_count = queries.shape[0]
    per_group = HEADS // KVH
    outputs = []
    for head in range(KVH):
        query_heads = queries[:, head * per_group * HD:(head + 1) * per_group * HD].reshape(
            row_count, per_group, HD
        )
        key_head = key_rows[:, head * HD:(head + 1) * HD]
        value_head = value_rows[:, head * HD:(head + 1) * HD]
        scores = jnp.einsum(
            "tgd,sd->gts", query_heads, key_head, preferred_element_type=jnp.float32
        ) * HD ** (-0.5)
        scores = jnp.where(allowed[None], scores, NEGATIVE)
        maxima = jnp.max(scores, axis=2, keepdims=True)
        weights = jnp.exp(scores - maxima)
        totals = jnp.sum(weights, axis=2)
        context = jnp.einsum(
            "gts,sd->tgd",
            weights.astype(jnp.bfloat16),
            value_head,
            preferred_element_type=jnp.float32,
        )
        context = context / jnp.transpose(totals)[..., None]
        outputs.append(context.reshape(row_count, per_group * HD))
    return jnp.concatenate(outputs, axis=1).astype(jnp.bfloat16)


def shards(
    hidden_in,
    queries,
    keys_new,
    values_new,
    keys_cache,
    values_cache,
    out_weight,
    norm_gain,
    gate_weight,
    up_weight,
    down_weight,
    lengths,
    slot_request,
    cache_group,
):
    owners = lax.axis_size("req")
    columns = lax.axis_size("mlp")
    owner_index = lax.axis_index("req")
    column_index = lax.axis_index("mlp")
    tokens = queries.shape[0]
    width_kv = keys_cache.shape[1]
    piece_rows = keys_cache.shape[0] // GROUPS
    slot_group = slot_request // (slot_request.shape[0] // GROUPS)
    own_row = cache_group[owner_index]
    wanted = lax.dynamic_slice_in_dim(slot_group.reshape(owners, columns), column_index, 1, 1)[:, 0]
    group_ids = jnp.arange(GROUPS, dtype=jnp.int32)
    sub_block = jnp.sum(
        jnp.where(own_row[None, :] == wanted[:, None], group_ids[None, :], 0), axis=1
    )
    slab_both = jnp.concatenate(
        [keys_cache.reshape(GROUPS, piece_rows, width_kv), values_cache.reshape(GROUPS, piece_rows, width_kv)],
        axis=2,
    )
    pick = (sub_block[:, None] == group_ids[None, :])[:, :, None, None]
    send_both = jnp.sum(jnp.where(pick, slab_both[None], jnp.zeros((), slab_both.dtype)), axis=1)
    got_both = lax.all_to_all(send_both, "req", split_axis=0, concat_axis=0, tiled=True)
    got_both = got_both.reshape(owners * piece_rows, 2 * width_kv)
    key_rows = jnp.concatenate([got_both[:, :width_kv], keys_new], axis=0)
    value_rows = jnp.concatenate([got_both[:, width_kv:], values_new], axis=0)
    positions = jnp.arange(tokens, dtype=jnp.int32)
    causal = positions[:, None] >= positions[None, :]
    allowed = jnp.concatenate(
        [jnp.ones((tokens, owners * piece_rows), jnp.bool_), causal], axis=1
    )
    context = full_attention(queries, key_rows, value_rows, allowed)
    attended = jnp.dot(context, out_weight, preferred_element_type=jnp.float32)
    residual = (hidden_in.astype(jnp.float32) + attended).astype(jnp.bfloat16)
    widened = residual.astype(jnp.float32)
    normed = (
        widened
        * lax.rsqrt(jnp.mean(widened * widened, axis=1, keepdims=True) + EPSILON)
        * norm_gain[None, :]
    ).astype(jnp.bfloat16)
    shard_rows = lax.all_gather(normed, "mlp", axis=0, tiled=True)
    block_width = gate_weight.shape[1]
    both_weights = jnp.concatenate([gate_weight, up_weight], axis=1)
    both_values = jnp.dot(shard_rows, both_weights, preferred_element_type=jnp.float32)
    gate_values = both_values[:, :block_width]
    upward = both_values[:, block_width:]
    hidden = (jax.nn.silu(gate_values) * upward).astype(jnp.bfloat16)
    partial_terms = jnp.dot(hidden, down_weight, preferred_element_type=jnp.float32)
    mixed = lax.psum_scatter(
        partial_terms.astype(jnp.bfloat16), "mlp", scatter_dimension=0, tiled=True
    ).astype(jnp.float32)
    result = residual.astype(jnp.float32) + mixed
    live_slot = positions[:, None] < lengths[0, 0]
    return jnp.where(live_slot, result, 0.0).astype(jnp.bfloat16)


def solution(mesh):
    return jax.shard_map(
        shards,
        mesh=mesh,
        in_specs=(
            P(("req", "mlp"), None),
            P(("req", "mlp"), None),
            P(("req", "mlp"), None),
            P(("req", "mlp"), None),
            P("req", None),
            P("req", None),
            P(),
            P(),
            P(None, "mlp"),
            P(None, "mlp"),
            P("mlp", None),
            P("req", "mlp"),
            P(),
            P(),
        ),
        out_specs=P(("req", "mlp"), None),
        check_vma=False,
    )
```

```python
import jax
import jax.numpy as jnp
from jax import lax
from jax.sharding import PartitionSpec as P

HEADS = 16
KVH = 4
HD = 128
GROUPS = 4


NEGATIVE = -1e30
EPSILON = 1e-06


def full_attention(queries, key_rows, value_rows, allowed):
    row_count = queries.shape[0]
    per_group = HEADS // KVH
    outputs = []
    for head in range(KVH):
        query_heads = queries[:, head * per_group * HD:(head + 1) * per_group * HD].reshape(
            row_count, per_group, HD
        )
        key_head = key_rows[:, head * HD:(head + 1) * HD]
        value_head = value_rows[:, head * HD:(head + 1) * HD]
        scores = jnp.einsum(
            "tgd,sd->gts", query_heads, key_head, preferred_element_type=jnp.float32
        ) * HD ** (-0.5)
        scores = jnp.where(allowed[None], scores, NEGATIVE)
        maxima = jnp.max(scores, axis=2, keepdims=True)
        weights = jnp.exp(scores - maxima)
        totals = jnp.sum(weights, axis=2)
        context = jnp.einsum(
            "gts,sd->tgd",
            weights.astype(jnp.bfloat16),
            value_head,
            preferred_element_type=jnp.float32,
        )
        context = context / jnp.transpose(totals)[..., None]
        outputs.append(context.reshape(row_count, per_group * HD))
    return jnp.concatenate(outputs, axis=1).astype(jnp.bfloat16)


def shards(
    hidden_in,
    queries,
    keys_new,
    values_new,
    keys_cache,
    values_cache,
    out_weight,
    norm_gain,
    gate_weight,
    up_weight,
    down_weight,
    lengths,
    slot_request,
    cache_group,
):
    owners = lax.axis_size("req")
    columns = lax.axis_size("mlp")
    owner_index = lax.axis_index("req")
    column_index = lax.axis_index("mlp")
    tokens = queries.shape[0]
    width_kv = keys_cache.shape[1]
    piece_rows = keys_cache.shape[0] // GROUPS
    slot_group = lax.div(slot_request, slot_request.shape[0] // GROUPS)
    own_row = cache_group[owner_index]
    wanted = lax.dynamic_slice_in_dim(slot_group.reshape(owners, columns), column_index, 1, 1)[:, 0]
    group_ids = jnp.arange(GROUPS, dtype=jnp.int32)
    sub_block = jnp.sum(
        jnp.where(own_row[None, :] == wanted[:, None], group_ids[None, :], 0), axis=1
    )
    slab_keys = keys_cache.reshape(GROUPS, piece_rows, width_kv)
    slab_values = values_cache.reshape(GROUPS, piece_rows, width_kv)
    pick = (sub_block[:, None] == group_ids[None, :])[:, :, None, None]
    zero = jnp.zeros((), keys_cache.dtype)
    send_keys = sum(jnp.where(pick[:, j], slab_keys[j][None], zero) for j in range(GROUPS))
    send_values = sum(jnp.where(pick[:, j], slab_values[j][None], zero) for j in range(GROUPS))
    send_both = jnp.concatenate([send_keys, send_values], axis=2)
    got_both = lax.all_to_all(send_both, "req", split_axis=0, concat_axis=0, tiled=True)
    got_both = got_both.reshape(owners * piece_rows, 2 * width_kv)
    key_rows = jnp.concatenate([got_both[:, :width_kv], keys_new], axis=0)
    value_rows = jnp.concatenate([got_both[:, width_kv:], values_new], axis=0)
    positions = jnp.arange(tokens, dtype=jnp.int32)
    causal = positions[:, None] >= positions[None, :]
    allowed = jnp.concatenate(
        [jnp.ones((tokens, owners * piece_rows), jnp.bool_), causal], axis=1
    )
    context = full_attention(queries, key_rows, value_rows, allowed)
    attended = jnp.dot(context, out_weight, preferred_element_type=jnp.float32)
    residual = (hidden_in.astype(jnp.float32) + attended).astype(jnp.bfloat16)
    widened = residual.astype(jnp.float32)
    normed = (
        widened
        * lax.rsqrt(jnp.mean(widened * widened, axis=1, keepdims=True) + EPSILON)
        * norm_gain[None, :]
    ).astype(jnp.bfloat16)
    shard_rows = lax.all_gather(normed, "mlp", axis=0, tiled=True)
    block_width = gate_weight.shape[1]
    both_weights = jnp.concatenate([gate_weight, up_weight], axis=1)
    both_values = jnp.dot(shard_rows, both_weights, preferred_element_type=jnp.float32)
    gate_values = both_values[:, :block_width]
    upward = both_values[:, block_width:]
    hidden = (jax.nn.silu(gate_values) * upward).astype(jnp.bfloat16)
    partial_terms = jnp.dot(hidden, down_weight, preferred_element_type=jnp.float32)
    mixed = lax.psum_scatter(
        partial_terms.astype(jnp.bfloat16), "mlp", scatter_dimension=0, tiled=True
    ).astype(jnp.float32)
    result = residual.astype(jnp.float32) + mixed
    live_slot = positions[:, None] < lengths[0, 0]
    return jnp.where(live_slot, result, 0.0).astype(jnp.bfloat16)


def solution(mesh):
    return jax.shard_map(
        shards,
        mesh=mesh,
        in_specs=(
            P(("req", "mlp"), None),
            P(("req", "mlp"), None),
            P(("req", "mlp"), None),
            P(("req", "mlp"), None),
            P("req", None),
            P("req", None),
            P(),
            P(),
            P(None, "mlp"),
            P(None, "mlp"),
            P("mlp", None),
            P("req", "mlp"),
            P(),
            P(),
        ),
        out_specs=P(("req", "mlp"), None),
        check_vma=False,
    )
```

```python
import jax
import jax.numpy as jnp
from jax import lax
from jax.sharding import PartitionSpec as P

HEADS = 16
KVH = 4
HD = 128
GROUPS = 4


NEGATIVE = -1e30
EPSILON = 1e-06


def full_attention(queries, key_rows, value_rows, allowed):
    row_count = queries.shape[0]
    per_group = HEADS // KVH
    outputs = []
    for head in range(KVH):
        query_heads = queries[:, head * per_group * HD:(head + 1) * per_group * HD].reshape(
            row_count, per_group, HD
        )
        key_head = key_rows[:, head * HD:(head + 1) * HD]
        value_head = value_rows[:, head * HD:(head + 1) * HD]
        scores = jnp.einsum(
            "tgd,sd->gts", query_heads, key_head, preferred_element_type=jnp.float32
        ) * HD ** (-0.5)
        scores = jnp.where(allowed[None], scores, NEGATIVE)
        maxima = jnp.max(scores, axis=2, keepdims=True)
        weights = jnp.exp(scores - maxima)
        totals = jnp.sum(weights, axis=2)
        context = jnp.einsum(
            "gts,sd->tgd",
            weights.astype(jnp.bfloat16),
            value_head,
            preferred_element_type=jnp.float32,
        )
        context = context / jnp.transpose(totals)[..., None]
        outputs.append(context.reshape(row_count, per_group * HD))
    return jnp.concatenate(outputs, axis=1).astype(jnp.bfloat16)


def shards(
    hidden_in,
    queries,
    keys_new,
    values_new,
    keys_cache,
    values_cache,
    out_weight,
    norm_gain,
    gate_weight,
    up_weight,
    down_weight,
    lengths,
    slot_request,
    cache_group,
):
    owners = lax.axis_size("req")
    columns = lax.axis_size("mlp")
    owner_index = lax.axis_index("req")
    column_index = lax.axis_index("mlp")
    tokens = queries.shape[0]
    width_kv = keys_cache.shape[1]
    piece_rows = keys_cache.shape[0] // GROUPS
    slot_group = lax.div(slot_request, slot_request.shape[0] // GROUPS)
    own_row = cache_group[owner_index]
    wanted = lax.dynamic_slice_in_dim(slot_group.reshape(owners, columns), column_index, 1, 1)[:, 0]
    group_ids = jnp.arange(GROUPS, dtype=jnp.int32)
    sub_block = jnp.sum(
        jnp.where(own_row[None, :] == wanted[:, None], group_ids[None, :], 0), axis=1
    )
    slab_keys = keys_cache.reshape(GROUPS, piece_rows, width_kv)
    slab_values = values_cache.reshape(GROUPS, piece_rows, width_kv)
    pick = (sub_block[:, None] == group_ids[None, :])[:, :, None, None]
    zero = jnp.zeros((), keys_cache.dtype)
    send_keys = sum(jnp.where(pick[:, j], slab_keys[j][None], zero) for j in range(GROUPS))
    send_values = sum(jnp.where(pick[:, j], slab_values[j][None], zero) for j in range(GROUPS))
    send_both = jnp.concatenate([send_keys, send_values], axis=1)
    got_both = lax.all_to_all(send_both, "req", split_axis=0, concat_axis=0, tiled=True)
    key_rows = jnp.concatenate(
        [got_both[:, :piece_rows].reshape(owners * piece_rows, width_kv), keys_new], axis=0
    )
    value_rows = jnp.concatenate(
        [got_both[:, piece_rows:].reshape(owners * piece_rows, width_kv), values_new], axis=0
    )
    positions = jnp.arange(tokens, dtype=jnp.int32)
    causal = positions[:, None] >= positions[None, :]
    allowed = jnp.concatenate(
        [jnp.ones((tokens, owners * piece_rows), jnp.bool_), causal], axis=1
    )
    context = full_attention(queries, key_rows, value_rows, allowed)
    attended = jnp.dot(context, out_weight, preferred_element_type=jnp.float32)
    residual = (hidden_in.astype(jnp.float32) + attended).astype(jnp.bfloat16)
    widened = residual.astype(jnp.float32)
    normed = (
        widened
        * lax.rsqrt(jnp.mean(widened * widened, axis=1, keepdims=True) + EPSILON)
        * norm_gain[None, :]
    ).astype(jnp.bfloat16)
    shard_rows = lax.all_gather(normed, "mlp", axis=0, tiled=True)
    block_width = gate_weight.shape[1]
    both_weights = jnp.concatenate([gate_weight, up_weight], axis=1)
    both_values = jnp.dot(shard_rows, both_weights, preferred_element_type=jnp.float32)
    gate_values = both_values[:, :block_width]
    upward = both_values[:, block_width:]
    hidden = (jax.nn.silu(gate_values) * upward).astype(jnp.bfloat16)
    partial_terms = jnp.dot(hidden, down_weight, preferred_element_type=jnp.float32)
    mixed = lax.psum_scatter(
        partial_terms.astype(jnp.bfloat16), "mlp", scatter_dimension=0, tiled=True
    ).astype(jnp.float32)
    live_slot = positions[:, None] < lengths[0, 0]
    kept = jnp.where(live_slot, residual.astype(jnp.float32), 0.0)
    live_scale = live_slot.astype(jnp.float32)
    return (kept + live_scale * mixed).astype(jnp.bfloat16)


def solution(mesh):
    return jax.shard_map(
        shards,
        mesh=mesh,
        in_specs=(
            P(("req", "mlp"), None),
            P(("req", "mlp"), None),
            P(("req", "mlp"), None),
            P(("req", "mlp"), None),
            P("req", None),
            P("req", None),
            P(),
            P(),
            P(None, "mlp"),
            P(None, "mlp"),
            P("mlp", None),
            P("req", "mlp"),
            P(),
            P(),
        ),
        out_specs=P(("req", "mlp"), None),
        check_vma=False,
    )
```

```python
import jax
import jax.numpy as jnp
from jax import lax
from jax.sharding import PartitionSpec as P

HEADS = 16
KVH = 4
HD = 128
GROUPS = 4


NEGATIVE = -1e30
EPSILON = 1e-06


def full_attention(queries, prefix_keys, prefix_values, keys_new, values_new, causal):
    row_count = queries.shape[0]
    per_group = HEADS // KVH
    outputs = []
    for head in range(KVH):
        columns = slice(head * HD, (head + 1) * HD)
        query_heads = queries[:, head * per_group * HD:(head + 1) * per_group * HD].reshape(
            row_count, per_group, HD
        )
        scores_new = jnp.einsum(
            "tgd,sd->gts", query_heads, keys_new[:, columns], preferred_element_type=jnp.float32
        ) * HD ** (-0.5)
        scores_new = jnp.where(causal[None], scores_new, NEGATIVE)
        scores_old = jnp.einsum(
            "tgd,sd->gts", query_heads, prefix_keys[:, columns], preferred_element_type=jnp.float32
        ) * HD ** (-0.5)
        maxima = jnp.maximum(
            jnp.max(scores_new, axis=2, keepdims=True), jnp.max(scores_old, axis=2, keepdims=True)
        )
        weights_new = jnp.exp(scores_new - maxima)
        weights_old = jnp.exp(scores_old - maxima)
        totals = jnp.sum(weights_new, axis=2) + jnp.sum(weights_old, axis=2)
        context = jnp.einsum(
            "gts,sd->tgd", weights_old.astype(jnp.bfloat16), prefix_values[:, columns],
            preferred_element_type=jnp.float32,
        ) + jnp.einsum(
            "gts,sd->tgd", weights_new.astype(jnp.bfloat16), values_new[:, columns],
            preferred_element_type=jnp.float32,
        )
        context = context / jnp.transpose(totals)[..., None]
        outputs.append(context.reshape(row_count, per_group * HD))
    return jnp.concatenate(outputs, axis=1).astype(jnp.bfloat16)


def shards(
    hidden_in,
    queries,
    keys_new,
    values_new,
    keys_cache,
    values_cache,
    out_weight,
    norm_gain,
    gate_weight,
    up_weight,
    down_weight,
    lengths,
    slot_request,
    cache_group,
):
    owners = lax.axis_size("req")
    columns = lax.axis_size("mlp")
    owner_index = lax.axis_index("req")
    column_index = lax.axis_index("mlp")
    tokens = queries.shape[0]
    width_kv = keys_cache.shape[1]
    piece_rows = keys_cache.shape[0] // GROUPS
    slot_group = lax.div(slot_request, slot_request.shape[0] // GROUPS)
    own_row = cache_group[owner_index]
    wanted = lax.dynamic_slice_in_dim(slot_group.reshape(owners, columns), column_index, 1, 1)[:, 0]
    group_ids = jnp.arange(GROUPS, dtype=jnp.int32)
    sub_block = jnp.sum(
        jnp.where(own_row[None, :] == wanted[:, None], group_ids[None, :], 0), axis=1
    )
    slab_keys = keys_cache.reshape(GROUPS, piece_rows, width_kv)
    slab_values = values_cache.reshape(GROUPS, piece_rows, width_kv)
    pick = (sub_block[:, None] == group_ids[None, :])[:, :, None, None]
    zero = jnp.zeros((), keys_cache.dtype)
    send_keys = sum(jnp.where(pick[:, j], slab_keys[j][None], zero) for j in range(GROUPS))
    send_values = sum(jnp.where(pick[:, j], slab_values[j][None], zero) for j in range(GROUPS))
    send_both = jnp.concatenate([send_keys, send_values], axis=2)
    got_both = lax.all_to_all(send_both, "req", split_axis=0, concat_axis=0, tiled=True)
    got_both = got_both.reshape(owners * piece_rows, 2 * width_kv)
    positions = jnp.arange(tokens, dtype=jnp.int32)
    causal = positions[:, None] >= positions[None, :]
    context = full_attention(
        queries, got_both[:, :width_kv], got_both[:, width_kv:], keys_new, values_new, causal
    )
    attended = jnp.dot(context, out_weight, preferred_element_type=jnp.float32)
    residual = (hidden_in.astype(jnp.float32) + attended).astype(jnp.bfloat16)
    widened = residual.astype(jnp.float32)
    normed = (
        widened
        * lax.rsqrt(jnp.mean(widened * widened, axis=1, keepdims=True) + EPSILON)
        * norm_gain[None, :]
    ).astype(jnp.bfloat16)
    shard_rows = lax.all_gather(normed, "mlp", axis=0, tiled=True)
    block_width = gate_weight.shape[1]
    both_weights = jnp.concatenate([gate_weight, up_weight], axis=1)
    both_values = jnp.dot(shard_rows, both_weights, preferred_element_type=jnp.float32)
    gate_values = both_values[:, :block_width]
    upward = both_values[:, block_width:]
    hidden = (jax.nn.silu(gate_values) * upward).astype(jnp.bfloat16)
    partial_terms = jnp.dot(hidden, down_weight, preferred_element_type=jnp.float32)
    mixed = lax.psum_scatter(
        partial_terms.astype(jnp.bfloat16), "mlp", scatter_dimension=0, tiled=True
    ).astype(jnp.float32)
    result = residual.astype(jnp.float32) + mixed
    live_slot = positions[:, None] < lengths[0, 0]
    return jnp.where(live_slot, result, 0.0).astype(jnp.bfloat16)


def solution(mesh):
    return jax.shard_map(
        shards,
        mesh=mesh,
        in_specs=(
            P(("req", "mlp"), None),
            P(("req", "mlp"), None),
            P(("req", "mlp"), None),
            P(("req", "mlp"), None),
            P("req", None),
            P("req", None),
            P(),
            P(),
            P(None, "mlp"),
            P(None, "mlp"),
            P("mlp", None),
            P("req", "mlp"),
            P(),
            P(),
        ),
        out_specs=P(("req", "mlp"), None),
        check_vma=False,
    )
```

```python
import jax
import jax.numpy as jnp
from jax import lax
from jax.sharding import PartitionSpec as P

HEADS = 16
KVH = 4
HD = 128
GROUPS = 4


NEGATIVE = -1e30
EPSILON = 1e-06


def full_attention(queries, key_rows, value_rows, allowed):
    row_count = queries.shape[0]
    per_group = HEADS // KVH
    outputs = []
    for head in range(KVH):
        query_heads = queries[:, head * per_group * HD:(head + 1) * per_group * HD].reshape(
            row_count, per_group, HD
        )
        key_head = key_rows[:, head * HD:(head + 1) * HD]
        value_head = value_rows[:, head * HD:(head + 1) * HD]
        scores = jnp.einsum(
            "tgd,sd->gts", query_heads, key_head, preferred_element_type=jnp.float32
        ) * HD ** (-0.5)
        scores = jnp.where(allowed[None], scores, NEGATIVE)
        maxima = jnp.max(scores, axis=2, keepdims=True)
        weights = jnp.exp(scores - maxima)
        totals = jnp.sum(weights, axis=2)
        context = jnp.einsum(
            "gts,sd->tgd",
            weights.astype(jnp.bfloat16),
            value_head,
            preferred_element_type=jnp.float32,
        )
        context = context / jnp.transpose(totals)[..., None]
        outputs.append(context.reshape(row_count, per_group * HD))
    return jnp.concatenate(outputs, axis=1).astype(jnp.bfloat16)


def shards(
    hidden_in,
    queries,
    keys_new,
    values_new,
    keys_cache,
    values_cache,
    out_weight,
    norm_gain,
    gate_weight,
    up_weight,
    down_weight,
    lengths,
    slot_request,
    cache_group,
):
    owners = lax.axis_size("req")
    columns = lax.axis_size("mlp")
    owner_index = lax.axis_index("req")
    column_index = lax.axis_index("mlp")
    tokens = queries.shape[0]
    width_kv = keys_cache.shape[1]
    piece_rows = keys_cache.shape[0] // GROUPS
    slot_group = lax.div(slot_request, slot_request.shape[0] // GROUPS)
    own_row = cache_group[owner_index]
    wanted = lax.dynamic_slice_in_dim(slot_group.reshape(owners, columns), column_index, 1, 1)[:, 0]
    group_ids = jnp.arange(GROUPS, dtype=jnp.int32)
    sub_block = jnp.sum(
        jnp.where(own_row[None, :] == wanted[:, None], group_ids[None, :], 0), axis=1
    )
    slab_keys = keys_cache.reshape(GROUPS, piece_rows, width_kv)
    slab_values = values_cache.reshape(GROUPS, piece_rows, width_kv)
    pick = (sub_block[:, None] == group_ids[None, :])[:, :, None, None]
    zero = jnp.zeros((), keys_cache.dtype)
    send_keys = sum(jnp.where(pick[:, j], slab_keys[j][None], zero) for j in range(GROUPS))
    send_values = sum(jnp.where(pick[:, j], slab_values[j][None], zero) for j in range(GROUPS))
    got_keys = lax.all_to_all(send_keys, "req", split_axis=0, concat_axis=0, tiled=True)
    got_values = lax.all_to_all(send_values, "req", split_axis=0, concat_axis=0, tiled=True)
    key_rows = jnp.concatenate(
        [got_keys.reshape(owners * piece_rows, width_kv), keys_new], axis=0
    )
    value_rows = jnp.concatenate(
        [got_values.reshape(owners * piece_rows, width_kv), values_new], axis=0
    )
    positions = jnp.arange(tokens, dtype=jnp.int32)
    causal = positions[:, None] >= positions[None, :]
    allowed = jnp.concatenate(
        [jnp.ones((tokens, owners * piece_rows), jnp.bool_), causal], axis=1
    )
    context = full_attention(queries, key_rows, value_rows, allowed)
    attended = jnp.dot(context, out_weight, preferred_element_type=jnp.float32)
    residual = (hidden_in.astype(jnp.float32) + attended).astype(jnp.bfloat16)
    widened = residual.astype(jnp.float32)
    normed = (
        widened
        * lax.rsqrt(jnp.mean(widened * widened, axis=1, keepdims=True) + EPSILON)
        * norm_gain[None, :]
    ).astype(jnp.bfloat16)
    shard_rows = lax.all_gather(normed, "mlp", axis=0, tiled=True)
    block_width = gate_weight.shape[1]
    both_weights = jnp.concatenate([gate_weight, up_weight], axis=1)
    both_values = jnp.dot(shard_rows, both_weights, preferred_element_type=jnp.float32)
    gate_values = both_values[:, :block_width]
    upward = both_values[:, block_width:]
    hidden = (jax.nn.silu(gate_values) * upward).astype(jnp.bfloat16)
    partial_terms = jnp.dot(hidden, down_weight, preferred_element_type=jnp.float32)
    mixed = lax.psum_scatter(
        partial_terms.astype(jnp.bfloat16), "mlp", scatter_dimension=0, tiled=True
    ).astype(jnp.float32)
    result = residual.astype(jnp.float32) + mixed
    live_slot = positions[:, None] < lengths[0, 0]
    return jnp.where(live_slot, result, 0.0).astype(jnp.bfloat16)


def solution(mesh):
    return jax.shard_map(
        shards,
        mesh=mesh,
        in_specs=(
            P(("req", "mlp"), None),
            P(("req", "mlp"), None),
            P(("req", "mlp"), None),
            P(("req", "mlp"), None),
            P("req", None),
            P("req", None),
            P(),
            P(),
            P(None, "mlp"),
            P(None, "mlp"),
            P("mlp", None),
            P("req", "mlp"),
            P(),
            P(),
        ),
        out_specs=P(("req", "mlp"), None),
        check_vma=False,
    )
```

```python
import jax
import jax.numpy as jnp
from jax import lax
from jax.sharding import PartitionSpec as P

HEADS = 16
KVH = 4
HD = 128
GROUPS = 4


NEGATIVE = -1e30
EPSILON = 1e-06


def full_attention(queries, key_rows, value_rows, allowed):
    row_count = queries.shape[0]
    per_group = HEADS // KVH
    outputs = []
    for head in range(KVH):
        query_heads = queries[:, head * per_group * HD:(head + 1) * per_group * HD].reshape(
            row_count, per_group, HD
        )
        key_head = key_rows[:, head * HD:(head + 1) * HD]
        value_head = value_rows[:, head * HD:(head + 1) * HD]
        scores = jnp.einsum(
            "tgd,sd->gts", query_heads, key_head, preferred_element_type=jnp.float32
        ) * HD ** (-0.5)
        scores = jnp.where(allowed[None], scores, NEGATIVE)
        maxima = jnp.max(scores, axis=2, keepdims=True)
        weights = jnp.exp(scores - maxima)
        totals = jnp.sum(weights, axis=2)
        context = jnp.einsum(
            "gts,sd->tgd",
            weights.astype(jnp.bfloat16),
            value_head,
            preferred_element_type=jnp.float32,
        )
        context = context / jnp.transpose(totals)[..., None]
        outputs.append(context.reshape(row_count, per_group * HD))
    return jnp.concatenate(outputs, axis=1).astype(jnp.bfloat16)


def shards(
    hidden_in,
    queries,
    keys_new,
    values_new,
    keys_cache,
    values_cache,
    out_weight,
    norm_gain,
    gate_weight,
    up_weight,
    down_weight,
    lengths,
    slot_request,
    cache_group,
):
    owners = lax.axis_size("req")
    columns = lax.axis_size("mlp")
    owner_index = lax.axis_index("req")
    column_index = lax.axis_index("mlp")
    tokens = queries.shape[0]
    width_kv = keys_cache.shape[1]
    piece_rows = keys_cache.shape[0] // GROUPS
    slot_group = lax.div(slot_request, slot_request.shape[0] // GROUPS)
    own_row = cache_group[owner_index]
    wanted = lax.dynamic_slice_in_dim(slot_group.reshape(owners, columns), column_index, 1, 1)[:, 0]
    group_ids = jnp.arange(GROUPS, dtype=jnp.int32)
    sub_block = jnp.sum(
        jnp.where(own_row[None, :] == wanted[:, None], group_ids[None, :], 0), axis=1
    )
    slab_both = jnp.concatenate(
        [keys_cache.reshape(GROUPS, piece_rows, width_kv), values_cache.reshape(GROUPS, piece_rows, width_kv)],
        axis=2,
    )
    send_both = jnp.stack(
        [lax.dynamic_index_in_dim(slab_both, sub_block[r], 0, keepdims=False) for r in range(owners)]
    )
    got_both = lax.all_to_all(send_both, "req", split_axis=0, concat_axis=0, tiled=True)
    got_both = got_both.reshape(owners * piece_rows, 2 * width_kv)
    key_rows = jnp.concatenate([got_both[:, :width_kv], keys_new], axis=0)
    value_rows = jnp.concatenate([got_both[:, width_kv:], values_new], axis=0)
    positions = jnp.arange(tokens, dtype=jnp.int32)
    causal = positions[:, None] >= positions[None, :]
    allowed = jnp.concatenate(
        [jnp.ones((tokens, owners * piece_rows), jnp.bool_), causal], axis=1
    )
    context = full_attention(queries, key_rows, value_rows, allowed)
    attended = jnp.dot(context, out_weight, preferred_element_type=jnp.float32)
    residual = (hidden_in.astype(jnp.float32) + attended).astype(jnp.bfloat16)
    widened = residual.astype(jnp.float32)
    normed = (
        widened
        * lax.rsqrt(jnp.mean(widened * widened, axis=1, keepdims=True) + EPSILON)
        * norm_gain[None, :]
    ).astype(jnp.bfloat16)
    shard_rows = lax.all_gather(normed, "mlp", axis=0, tiled=True)
    block_width = gate_weight.shape[1]
    both_weights = jnp.concatenate([gate_weight, up_weight], axis=1)
    both_values = jnp.dot(shard_rows, both_weights, preferred_element_type=jnp.float32)
    gate_values = both_values[:, :block_width]
    upward = both_values[:, block_width:]
    hidden = (jax.nn.silu(gate_values) * upward).astype(jnp.bfloat16)
    partial_terms = jnp.dot(hidden, down_weight, preferred_element_type=jnp.float32)
    mixed = lax.psum_scatter(
        partial_terms.astype(jnp.bfloat16), "mlp", scatter_dimension=0, tiled=True
    ).astype(jnp.float32)
    result = residual.astype(jnp.float32) + mixed
    live_slot = positions[:, None] < lengths[0, 0]
    return jnp.where(live_slot, result, 0.0).astype(jnp.bfloat16)


def solution(mesh):
    return jax.shard_map(
        shards,
        mesh=mesh,
        in_specs=(
            P(("req", "mlp"), None),
            P(("req", "mlp"), None),
            P(("req", "mlp"), None),
            P(("req", "mlp"), None),
            P("req", None),
            P("req", None),
            P(),
            P(),
            P(None, "mlp"),
            P(None, "mlp"),
            P("mlp", None),
            P("req", "mlp"),
            P(),
            P(),
        ),
        out_specs=P(("req", "mlp"), None),
        check_vma=False,
    )
```

```python
import jax
import jax.numpy as jnp
from jax import lax
from jax.sharding import PartitionSpec as P

HEADS = 16
KVH = 4
HD = 128
GROUPS = 4


NEGATIVE = -1e30
EPSILON = 1e-06


def full_attention(queries, key_rows, value_rows, allowed):
    row_count = queries.shape[0]
    per_group = HEADS // KVH
    outputs = []
    for head in range(KVH):
        query_heads = queries[:, head * per_group * HD:(head + 1) * per_group * HD].reshape(
            row_count, per_group, HD
        )
        key_head = key_rows[:, head * HD:(head + 1) * HD]
        value_head = value_rows[:, head * HD:(head + 1) * HD]
        scores = jnp.einsum(
            "tgd,sd->gts", query_heads, key_head, preferred_element_type=jnp.float32
        ) * HD ** (-0.5)
        scores = jnp.where(allowed[None], scores, NEGATIVE)
        maxima = jnp.max(scores, axis=2, keepdims=True)
        weights = jnp.exp(scores - maxima)
        totals = jnp.sum(weights, axis=2)
        context = jnp.einsum(
            "gts,sd->tgd",
            weights.astype(jnp.bfloat16),
            value_head,
            preferred_element_type=jnp.float32,
        )
        context = context / jnp.transpose(totals)[..., None]
        outputs.append(context.reshape(row_count, per_group * HD))
    return jnp.concatenate(outputs, axis=1).astype(jnp.bfloat16)


def shards(
    hidden_in,
    queries,
    keys_new,
    values_new,
    keys_cache,
    values_cache,
    out_weight,
    norm_gain,
    gate_weight,
    up_weight,
    down_weight,
    lengths,
    slot_request,
    cache_group,
):
    owners = lax.axis_size("req")
    columns = lax.axis_size("mlp")
    owner_index = lax.axis_index("req")
    column_index = lax.axis_index("mlp")
    tokens = queries.shape[0]
    width_kv = keys_cache.shape[1]
    piece_rows = keys_cache.shape[0] // GROUPS
    slot_group = lax.div(slot_request, slot_request.shape[0] // GROUPS)
    own_row = cache_group[owner_index]
    wanted = lax.dynamic_slice_in_dim(slot_group.reshape(owners, columns), column_index, 1, 1)[:, 0]
    group_ids = jnp.arange(GROUPS, dtype=jnp.int32)
    sub_block = jnp.sum(
        jnp.where(own_row[None, :] == wanted[:, None], group_ids[None, :], 0), axis=1
    )
    slab_keys = keys_cache.reshape(GROUPS, piece_rows, width_kv)
    slab_values = values_cache.reshape(GROUPS, piece_rows, width_kv)
    pick = (sub_block[:, None] == group_ids[None, :])[:, :, None, None]
    zero = jnp.zeros((), keys_cache.dtype)
    send_keys = sum(jnp.where(pick[:, j], slab_keys[j][None], zero) for j in range(GROUPS))
    send_values = sum(jnp.where(pick[:, j], slab_values[j][None], zero) for j in range(GROUPS))
    send_both = jnp.concatenate([send_keys, send_values], axis=2)
    got_both = lax.all_to_all(send_both, "req", split_axis=0, concat_axis=0, tiled=True)
    got_both = got_both.reshape(owners * piece_rows, 2 * width_kv)
    key_rows = jnp.concatenate([got_both[:, :width_kv], keys_new], axis=0)
    value_rows = jnp.concatenate([got_both[:, width_kv:], values_new], axis=0)
    positions = jnp.arange(tokens, dtype=jnp.int32)
    causal = positions[:, None] >= positions[None, :]
    allowed = jnp.concatenate(
        [jnp.ones((tokens, owners * piece_rows), jnp.bool_), causal], axis=1
    )
    context = full_attention(queries, key_rows, value_rows, allowed)
    attended = jnp.dot(context, out_weight, preferred_element_type=jnp.float32)
    residual = (hidden_in.astype(jnp.float32) + attended).astype(jnp.bfloat16)
    widened = residual.astype(jnp.float32)
    normed = (
        widened
        * lax.rsqrt(jnp.mean(widened * widened, axis=1, keepdims=True) + EPSILON)
        * norm_gain[None, :]
    ).astype(jnp.bfloat16)
    shard_rows = lax.all_gather(normed, "mlp", axis=0, tiled=True)
    block_width = gate_weight.shape[1]
    both_weights = jnp.concatenate([gate_weight, up_weight], axis=1)
    both_values = jnp.dot(shard_rows, both_weights, preferred_element_type=jnp.float32)
    gate_values = both_values[:, :block_width]
    upward = both_values[:, block_width:]
    hidden = lax.optimization_barrier((jax.nn.silu(gate_values) * upward).astype(jnp.bfloat16))
    partial_terms = jnp.dot(hidden, down_weight, preferred_element_type=jnp.float32)
    mixed = lax.psum_scatter(
        partial_terms.astype(jnp.bfloat16), "mlp", scatter_dimension=0, tiled=True
    ).astype(jnp.float32)
    result = residual.astype(jnp.float32) + mixed
    live_slot = positions[:, None] < lengths[0, 0]
    return jnp.where(live_slot, result, 0.0).astype(jnp.bfloat16)


def solution(mesh):
    return jax.shard_map(
        shards,
        mesh=mesh,
        in_specs=(
            P(("req", "mlp"), None),
            P(("req", "mlp"), None),
            P(("req", "mlp"), None),
            P(("req", "mlp"), None),
            P("req", None),
            P("req", None),
            P(),
            P(),
            P(None, "mlp"),
            P(None, "mlp"),
            P("mlp", None),
            P("req", "mlp"),
            P(),
            P(),
        ),
        out_specs=P(("req", "mlp"), None),
        check_vma=False,
    )
```
